256 devices in a mesh: tm: 64 (over x, z_hi, y), tile: 4 (over z_lo, core).
Axes of the slice: x: 4, y: 4, z: 8 (z_hi: 4, z_lo: 2; z = z_hi * 2 + z_lo), core: 2. Of those that a mesh axis runs over, the one named last changes fastest.
Arguments:
- diag_blocks: float32 [128, 1024, 1024], P('tm', None, 'tile'), as said below
- upper_blocks: float32 [128, 1024, 1024], P('tm', None, 'tile')
- arrow_blocks: float32 [128, 64, 1024], P('tm')
- tip_block: float32 [64, 64], replicated, as said below
Outputs:
- red_diag: float32 [64, 1024, 1024], P(None, 'tm', 'tile')
- red_upper: float32 [64, 1024, 1024], P(None, 'tm', 'tile')
- red_arrow: float32 [64, 64, 1024], P('tm', None, 'tile')
- red_tip: float32 [64, 64], replicated
Inputs may be any that keep to these rules, and one draw needn't show every extreme that they name: `diag_blocks`: every diagonal block is symmetric, and Q is symmetric positive definite. `tip_block`: Symmetric.
All inputs are finite; a program needn't handle non-finite values.
Results may differ from the reference program's by a relative error of at most 0.00016.
Values sent between devices are 32-bit elements; how exact they have to be, the bound alone decides.
No kernel may reach another device: no remote copies, remote signals or barrier semaphores. Data moves between devices by JAX's collectives and lax.ppermute only.
A program may use at most 128 MiB of HBM per device.

```python
import math
import jax
import jax.numpy as jnp
from jax import lax

B = 1024
A = 64
K = 2
NT = 128
N_TM = 64


def mesh_laplacian(key_mesh):
    edge_weights = jax.random.uniform(key_mesh, (NT, B - 1), jnp.float32, 7.0, 13.0)
    zero_column = jnp.zeros((NT, 1), jnp.float32)
    weight_after = jnp.concatenate([edge_weights, zero_column], axis=1)
    weight_before = jnp.concatenate([zero_column, edge_weights], axis=1)
    node_degree = weight_after + weight_before
    neighbour = weight_after[:, :, None] * jnp.eye(B, k=1, dtype=jnp.float32)
    return node_degree[:, :, None] * jnp.eye(B, dtype=jnp.float32) - neighbour - jnp.swapaxes(neighbour, 1, 2)


def draw_diag_blocks(key, part):
    key_noise = jax.random.fold_in(key, 0)
    key_main = jax.random.fold_in(key, 1)
    key_mesh = jax.random.fold_in(key, 3)
    noise_part = jax.random.uniform(key_noise, (NT, B, B), jnp.float32, -1.0, 1.0) * 1.7320508
    noise_part = noise_part * (3.0 / math.sqrt(B))
    symmetric = (noise_part + jnp.swapaxes(noise_part, 1, 2)) * 0.70710678
    diagonal = jax.random.uniform(key_main, (NT, B), jnp.float32, 18.0, 24.0)
    return symmetric + diagonal[:, :, None] * jnp.eye(B, dtype=jnp.float32) + mesh_laplacian(key_mesh)


def draw_upper_blocks(key, part):
    key_noise, key_main = jax.random.split(key, 2)
    noise_part = jax.random.uniform(key_noise, (NT, B, B), jnp.float32, -1.0, 1.0) * 1.7320508
    noise_part = noise_part * (0.6 / math.sqrt(B))
    diagonal = -jax.random.uniform(key_main, (NT, B), jnp.float32, 1.5, 3.0)
    return noise_part + diagonal[:, :, None] * jnp.eye(B, dtype=jnp.float32)


def draw_arrow_blocks(key, part):
    key_noise = jax.random.fold_in(key, 0)
    noise_part = jax.random.uniform(key_noise, (NT, A, B), jnp.float32, -1.0, 1.0) * 1.7320508
    ramp = jnp.arange(NT, dtype=jnp.float32) / (NT - 1)
    scale = jnp.sqrt(60.0 * (1.0 + 2.0 * ramp) / (NT * B))
    return noise_part * scale[:, None, None]


def draw_tip_block(key, part):
    key_noise, key_main = jax.random.split(key, 2)
    noise_part = jax.random.uniform(key_noise, (A, A), jnp.float32, -1.0, 1.0) * 1.7320508
    noise_part = noise_part * (0.5 / math.sqrt(A))
    symmetric = (noise_part + noise_part.T) * 0.70710678
    diagonal = jax.random.uniform(key_main, (A,), jnp.float32, 20.0, 26.0)
    return symmetric + jnp.diag(diagonal)


def setup_inputs(seed: int = 0) -> dict:
    seeds = jax.random.split(jax.random.key(seed), 5)
    diag_blocks = draw_diag_blocks(jax.random.fold_in(seeds[4], 71), 0)
    upper_blocks = draw_upper_blocks(jax.random.fold_in(seeds[4], 71), 0)
    arrow_blocks = draw_arrow_blocks(jax.random.fold_in(seeds[4], 71), 0)
    tip_block = draw_tip_block(jax.random.fold_in(seeds[4], 71), 0)
    return {"diag_blocks": diag_blocks, "upper_blocks": upper_blocks, "arrow_blocks": arrow_blocks, "tip_block": tip_block}


precise = lax.Precision.HIGHEST

def lower_solve(factor, rhs):
    return lax.linalg.triangular_solve(factor, rhs, left_side=True, lower=True)

def product(left, right):
    return jnp.dot(left.T, right, precision=precise)

def eliminate(diag_part, upper_part, arrow_part, upper_after):
    top_diag = diag_part[0]
    top_arrow = arrow_part[0].T
    tip_part = jnp.zeros((A, A), jnp.float32)
    pivot_full = diag_part[1]
    fill_full = upper_part[1].T
    branch_cols = arrow_part[1].T
    for section in range(1, K):
        factor = jnp.linalg.cholesky(pivot_full)
        fill_solved = lower_solve(factor, fill_full)
        branch_solved = lower_solve(factor, branch_cols)
        top_diag = top_diag - product(fill_solved, fill_solved)
        top_arrow = top_arrow - product(fill_solved, branch_solved)
        tip_part = tip_part - product(branch_solved, branch_solved)
        if section + 1 < K:
            link_full = lower_solve(factor, upper_part[section + 1])
            pivot_full = diag_part[section + 1] - product(link_full, link_full)
            fill_full = -product(link_full, fill_solved)
            branch_cols = arrow_part[section + 1].T - product(link_full, branch_solved)
        else:
            link_full = lower_solve(factor, upper_after)
            next_diag = -product(link_full, link_full)
            next_upper = -product(fill_solved, link_full)
            next_arrow = -product(branch_solved, link_full)
    return (top_diag, top_arrow.T, tip_part, next_diag, next_upper, next_arrow)

def reference(diag_blocks, upper_blocks, arrow_blocks, tip_block):
    diag_parts = diag_blocks.reshape(N_TM, K, B, B)
    upper_parts = upper_blocks.reshape(N_TM, K, B, B)
    arrow_parts = arrow_blocks.reshape(N_TM, K, A, B)
    upper_after = jnp.concatenate([upper_parts[1:, 0], jnp.zeros((1, B, B), jnp.float32)], axis=0)

    def partition_step(pieces):
        return eliminate(pieces[0], pieces[1], pieces[2], pieces[3])
    results = lax.map(partition_step, (diag_parts, upper_parts, arrow_parts, upper_after))
    top_diag, top_arrow, tip_part, next_diag, next_upper, next_arrow = results
    zero_block = jnp.zeros((1, B, B), jnp.float32)
    red_diag = top_diag + jnp.concatenate([zero_block, next_diag[:-1]], axis=0)
    red_upper = jnp.concatenate([zero_block, next_upper[:-1]], axis=0)
    red_arrow = top_arrow + jnp.concatenate([jnp.zeros((1, A, B), jnp.float32), next_arrow[:-1]], axis=0)
    red_tip = tip_block + jnp.sum(tip_part, axis=0)
    return (red_diag, red_upper, red_arrow, red_tip)
```

```python
import jax
import jax.numpy as jnp
from jax import lax
from jax.sharding import PartitionSpec as P

precise = lax.Precision.HIGHEST


def shifted(value, axis, by):
    count = lax.axis_size(axis)
    pairs = [(i, i + by) for i in range(count) if 0 <= i + by < count]
    return lax.ppermute(value, axis, pairs)


def lower_solve(factor, rhs):
    return lax.linalg.triangular_solve(factor, rhs, left_side=True, lower=True)


def product(left, right):
    return jnp.dot(left.T, right, precision=precise)


def body(diag_blocks, upper_blocks, arrow_blocks, tip_block):
    strip_width = diag_blocks.shape[2]
    offset = lax.axis_index("tile") * strip_width
    upper_after = shifted(upper_blocks[0], "tm", -1)
    both_full = lax.all_gather(
        jnp.stack([diag_blocks[1], upper_blocks[1]]), "tile", axis=2, tiled=True)
    whole_pivot = both_full[0]
    first_full = both_full[1]
    fill_strip = lax.dynamic_slice_in_dim(first_full, offset, strip_width, 0).T
    top_diag = diag_blocks[0]
    top_arrow = arrow_blocks[0].T
    branch_cols = arrow_blocks[1].T
    factor = jnp.linalg.cholesky(whole_pivot)
    branch_solved = lower_solve(factor, branch_cols)
    tip_part = -product(branch_solved, branch_solved)
    tip_all = lax.all_gather(tip_part, "tm")
    fill_solved = lower_solve(factor, fill_strip)
    link_strip = lower_solve(factor, upper_after)
    solved_all = lax.all_gather(
        jnp.stack([link_strip, fill_solved]), "tile", axis=2, tiled=True)
    link_all = solved_all[0]
    fill_all = solved_all[1]
    top_diag = top_diag - product(fill_all, fill_solved)
    top_arrow = top_arrow - product(fill_all, branch_solved)
    next_diag = -product(link_all, link_strip)
    next_upper = -product(fill_all, link_strip)
    next_arrow = -product(branch_solved, link_strip)
    red_tip = tip_block + jnp.sum(tip_all, axis=0)
    own_arrow = lax.dynamic_slice_in_dim(top_arrow, offset, strip_width, 0).T
    came_diag, came_upper, came_arrow = shifted((next_diag, next_upper, next_arrow), "tm", 1)
    whole_diag = top_diag + came_diag
    stacked = jnp.stack([whole_diag, came_upper])[None]
    spread = lax.all_to_all(stacked, "tm", split_axis=2, concat_axis=0, tiled=True)
    red_diag = spread[:, 0]
    red_upper = spread[:, 1]
    red_arrow = (own_arrow + came_arrow)[None]
    return (red_diag, red_upper, red_arrow, red_tip)


def solution(mesh):
    return jax.shard_map(
        body,
        mesh=mesh,
        in_specs=(P("tm", None, "tile"), P("tm", None, "tile"), P("tm", None, None), P()),
        out_specs=(P(None, "tm", "tile"), P(None, "tm", "tile"), P("tm", None, "tile"), P()),
        check_vma=False,
    )
```

```python
import jax
import jax.numpy as jnp
from jax import lax
from jax.sharding import PartitionSpec as P

precise = lax.Precision.HIGHEST
BLOCK = 128


def shifted(value, axis, by):
    count = lax.axis_size(axis)
    pairs = [(i, i + by) for i in range(count) if 0 <= i + by < count]
    return lax.ppermute(value, axis, pairs)


def mm(left, right):
    return jnp.dot(left, right, precision=precise)


def product(left, right):
    return jnp.dot(left.T, right, precision=precise)


def full_columns(strips):
    tile = lax.axis_index("tile")
    count = lax.axis_size("tile")
    far = lax.ppermute(strips, "tile", [(j, j ^ 2) for j in range(count)])
    upper_chip = tile // 2 == 1
    low = jnp.where(upper_chip, far, strips)
    high = jnp.where(upper_chip, strips, far)
    mine = jnp.stack([low, high])
    other = lax.ppermute(mine, "tile", [(j, j ^ 1) for j in range(count)])
    second_core = tile % 2 == 1
    first = jnp.where(second_core, other, mine)
    second = jnp.where(second_core, mine, other)
    return jnp.concatenate([first[0], second[0], first[1], second[1]], axis=-1)


def factor_blocks(pivot):
    size = pivot.shape[0]
    eye = jnp.eye(BLOCK, dtype=pivot.dtype)
    inverses, panels = [], []
    rest = pivot
    for start in range(0, size, BLOCK):
        head = jnp.linalg.cholesky(rest[:BLOCK, :BLOCK])
        head_inv = lax.linalg.triangular_solve(head, eye, left_side=True, lower=True)
        inverses.append(head_inv)
        if start + BLOCK < size:
            below = mm(rest[BLOCK:, :BLOCK], head_inv.T)
            panels.append(below)
            rest = rest[BLOCK:, BLOCK:] - mm(below, below.T)
    return inverses, panels


def forward_solve(inverses, panels, rhs):
    solved = []
    rest = rhs
    for step, head_inv in enumerate(inverses):
        part = mm(head_inv, rest[:BLOCK])
        solved.append(part)
        if step < len(panels):
            rest = rest[BLOCK:] - mm(panels[step], part)
    return jnp.concatenate(solved, axis=0)


def body(diag_blocks, upper_blocks, arrow_blocks, tip_block):
    strip_width = diag_blocks.shape[2]
    nodes = diag_blocks.shape[1]
    offset = lax.axis_index("tile") * strip_width
    upper_after = shifted(upper_blocks[0], "tm", -1)
    whole_pivot = full_columns(diag_blocks[1])
    couplings = full_columns(jnp.stack([upper_blocks[1], upper_after]))
    first_full = couplings[0]
    next_full = couplings[1]
    inverses, panels = factor_blocks(whole_pivot)
    rhs = jnp.concatenate([first_full.T, next_full, arrow_blocks[1].T], axis=1)
    solved = forward_solve(inverses, panels, rhs)
    fill_all = solved[:, :nodes]
    link_all = solved[:, nodes:2 * nodes]
    branch_solved = solved[:, 2 * nodes:]
    tip_part = -product(branch_solved, branch_solved)
    tip_all = lax.all_gather(tip_part, "tm")
    fill_strip = lax.dynamic_slice_in_dim(fill_all, offset, strip_width, 1)
    link_strip = lax.dynamic_slice_in_dim(link_all, offset, strip_width, 1)
    top_diag = diag_blocks[0] - product(fill_all, fill_strip)
    own_arrow = lax.dynamic_slice_in_dim(arrow_blocks[0], offset, strip_width, 1)
    own_arrow = own_arrow - product(branch_solved, fill_strip)
    next_diag = -product(link_all, link_strip)
    next_upper = -product(fill_all, link_strip)
    next_arrow = -product(branch_solved, link_strip)
    red_tip = tip_block + jnp.sum(tip_all, axis=0)
    came_diag, came_upper, came_arrow = shifted((next_diag, next_upper, next_arrow), "tm", 1)
    whole_diag = top_diag + came_diag
    stacked = jnp.stack([whole_diag, came_upper])[None]
    spread = lax.all_to_all(stacked, "tm", split_axis=2, concat_axis=0, tiled=True)
    red_diag = spread[:, 0]
    red_upper = spread[:, 1]
    red_arrow = (own_arrow + came_arrow)[None]
    return (red_diag, red_upper, red_arrow, red_tip)


def solution(mesh):
    return jax.shard_map(
        body,
        mesh=mesh,
        in_specs=(P("tm", None, "tile"), P("tm", None, "tile"), P("tm", None, None), P()),
        out_specs=(P(None, "tm", "tile"), P(None, "tm", "tile"), P("tm", None, "tile"), P()),
        check_vma=False,
    )
```

```python
import jax
import jax.numpy as jnp
from jax import lax
from jax.sharding import PartitionSpec as P

precise = lax.Precision.HIGHEST
BLOCK = 128


def shifted(value, axis, by):
    count = lax.axis_size(axis)
    pairs = [(i, i + by) for i in range(count) if 0 <= i + by < count]
    return lax.ppermute(value, axis, pairs)


def mm(left, right):
    return jnp.dot(left, right, precision=precise)


def product(left, right):
    return jnp.dot(left.T, right, precision=precise)


def chip_pair(strips):
    tile = lax.axis_index("tile")
    count = lax.axis_size("tile")
    far = lax.ppermute(strips, "tile", [(j, j ^ 2) for j in range(count)])
    upper_chip = tile // 2 == 1
    low = jnp.where(upper_chip, far, strips)
    high = jnp.where(upper_chip, strips, far)
    return jnp.stack([low, high])


def join_cores(mine):
    tile = lax.axis_index("tile")
    count = lax.axis_size("tile")
    other = lax.ppermute(mine, "tile", [(j, j ^ 1) for j in range(count)])
    second_core = tile % 2 == 1
    first = jnp.where(second_core, other, mine)
    second = jnp.where(second_core, mine, other)
    return jnp.concatenate([first[0], second[0], first[1], second[1]], axis=-1)


def full_columns(strips):
    return join_cores(chip_pair(strips))


def factor_blocks(pivot, riders, hooks):
    size = pivot.shape[0]
    eye = jnp.eye(BLOCK, dtype=pivot.dtype)
    inverses, panels = [], []
    rest = pivot
    for step, start in enumerate(range(0, size, BLOCK)):
        head = jnp.linalg.cholesky(rest[:BLOCK, :BLOCK])
        if step in hooks:
            head, riders = lax.optimization_barrier((head, riders))
            riders = hooks[step](riders)
        head_inv = lax.linalg.triangular_solve(head, eye, left_side=True, lower=True)
        inverses.append(head_inv)
        if start + BLOCK < size:
            below = mm(rest[BLOCK:, :BLOCK], head_inv.T)
            panels.append(below)
            rest = rest[BLOCK:, BLOCK:] - mm(below, below.T)
    return inverses, panels, riders


def forward_solve(inverses, panels, rhs):
    solved = []
    rest = rhs
    for step, head_inv in enumerate(inverses):
        part = mm(head_inv, rest[:BLOCK])
        solved.append(part)
        if step < len(panels):
            rest = rest[BLOCK:] - mm(panels[step], part)
    return jnp.concatenate(solved, axis=0)


def body(diag_blocks, upper_blocks, arrow_blocks, tip_block):
    strip_width = diag_blocks.shape[2]
    nodes = diag_blocks.shape[1]
    parts = lax.axis_size("tm")
    offset = lax.axis_index("tile") * strip_width
    whole_pivot = full_columns(diag_blocks[1])
    hooks = {
        0: lambda r: (chip_pair(r[0]), shifted(r[1], "tm", -1)),
        2: lambda r: (join_cores(r[0]), chip_pair(r[1])),
        4: lambda r: (r[0], join_cores(r[1])),
    }
    inverses, panels, riders = factor_blocks(
        whole_pivot, (upper_blocks[1], upper_blocks[0]), hooks)
    first_full, next_full = riders
    branch_solved = forward_solve(inverses, panels, arrow_blocks[1].T)
    tip_part = -product(branch_solved, branch_solved)
    tip_all = lax.all_gather(tip_part, "tm")
    rhs = jnp.concatenate([first_full.T, next_full], axis=1)
    solved = forward_solve(inverses, panels, rhs)
    fill_all = solved[:, :nodes]
    link_all = solved[:, nodes:]
    fill_strip = lax.dynamic_slice_in_dim(fill_all, offset, strip_width, 1)
    link_strip = lax.dynamic_slice_in_dim(link_all, offset, strip_width, 1)
    top_diag = diag_blocks[0] - product(fill_all, fill_strip)
    own_arrow = lax.dynamic_slice_in_dim(arrow_blocks[0], offset, strip_width, 1)
    own_arrow = own_arrow - product(branch_solved, fill_strip)
    next_arrow = -product(branch_solved, link_strip)
    came_arrow = shifted(next_arrow, "tm", 1)
    next_diag = -product(link_all, link_strip)
    next_upper = -product(fill_all, link_strip)
    stacked = jnp.stack([top_diag, next_diag, next_upper])[None]
    tip_all, stacked = lax.optimization_barrier((tip_all, stacked))
    spread = lax.all_to_all(stacked, "tm", split_axis=2, concat_axis=0, tiled=True)
    zero = jnp.zeros_like(spread[:1, 1])
    before = jnp.concatenate([zero, spread[:parts - 1, 1]], axis=0)
    red_diag = spread[:, 0] + before
    red_upper = jnp.concatenate([zero, spread[:parts - 1, 2]], axis=0)
    red_tip = tip_block + jnp.sum(tip_all, axis=0)
    red_arrow = (own_arrow + came_arrow)[None]
    return (red_diag, red_upper, red_arrow, red_tip)


def solution(mesh):
    return jax.shard_map(
        body,
        mesh=mesh,
        in_specs=(P("tm", None, "tile"), P("tm", None, "tile"), P("tm", None, None), P()),
        out_specs=(P(None, "tm", "tile"), P(None, "tm", "tile"), P("tm", None, "tile"), P()),
        check_vma=False,
    )
```

```python
import jax
import jax.numpy as jnp
from jax import lax
from jax.sharding import PartitionSpec as P

precise = lax.Precision.HIGHEST
BLOCK = 128


def shifted(value, axis, by):
    count = lax.axis_size(axis)
    pairs = [(i, i + by) for i in range(count) if 0 <= i + by < count]
    return lax.ppermute(value, axis, pairs)


def mm(left, right):
    return jnp.dot(left, right, precision=precise)


def product(left, right):
    return jnp.dot(left.T, right, precision=precise)


def chip_pair(strips):
    tile = lax.axis_index("tile")
    count = lax.axis_size("tile")
    far = lax.ppermute(strips, "tile", [(j, j ^ 2) for j in range(count)])
    upper_chip = tile // 2 == 1
    low = jnp.where(upper_chip, far, strips)
    high = jnp.where(upper_chip, strips, far)
    return jnp.stack([low, high])


def join_cores(mine):
    tile = lax.axis_index("tile")
    count = lax.axis_size("tile")
    other = lax.ppermute(mine, "tile", [(j, j ^ 1) for j in range(count)])
    second_core = tile % 2 == 1
    first = jnp.where(second_core, other, mine)
    second = jnp.where(second_core, mine, other)
    return jnp.concatenate([first[0], second[0], first[1], second[1]], axis=-1)


def full_columns(strips):
    return join_cores(chip_pair(strips))


def factor_blocks(pivot, riders, hooks):
    size = pivot.shape[0]
    eye = jnp.eye(BLOCK, dtype=pivot.dtype)
    inverses, panels = [], []
    rest = pivot
    for step, start in enumerate(range(0, size, BLOCK)):
        head = jnp.linalg.cholesky(rest[:BLOCK, :BLOCK])
        if step in hooks:
            head, riders = lax.optimization_barrier((head, riders))
            riders = hooks[step](riders)
        head_inv = lax.linalg.triangular_solve(head, eye, left_side=True, lower=True)
        inverses.append(head_inv)
        if start + BLOCK < size:
            below = mm(rest[BLOCK:, :BLOCK], head_inv.T)
            panels.append(below)
            rest = rest[BLOCK:, BLOCK:] - mm(below, below.T)
    return inverses, panels, riders


def forward_solve(inverses, panels, rhs):
    solved = []
    rest = rhs
    for step, head_inv in enumerate(inverses):
        part = mm(head_inv, rest[:BLOCK])
        solved.append(part)
        if step < len(panels):
            rest = rest[BLOCK:] - mm(panels[step], part)
    return jnp.concatenate(solved, axis=0)


def body(diag_blocks, upper_blocks, arrow_blocks, tip_block):
    strip_width = diag_blocks.shape[2]
    nodes = diag_blocks.shape[1]
    parts = lax.axis_size("tm")
    offset = lax.axis_index("tile") * strip_width
    whole_pivot = full_columns(diag_blocks[1])
    upper_after = shifted(upper_blocks[0], "tm", -1)
    hooks = {
        0: lambda r: (chip_pair(r[0]), chip_pair(r[1])),
        3: lambda r: (join_cores(r[0]), join_cores(r[1])),
    }
    inverses, panels, riders = factor_blocks(
        whole_pivot, (upper_blocks[1], upper_after), hooks)
    first_full, next_full = riders
    branch_solved = forward_solve(inverses, panels, arrow_blocks[1].T)
    tip_part = -product(branch_solved, branch_solved)
    tip_all = lax.all_gather(tip_part, "tm")
    rhs = jnp.concatenate([first_full.T, next_full], axis=1)
    solved = forward_solve(inverses, panels, rhs)
    fill_all = solved[:, :nodes]
    link_all = solved[:, nodes:]
    fill_strip = lax.dynamic_slice_in_dim(fill_all, offset, strip_width, 1)
    link_strip = lax.dynamic_slice_in_dim(link_all, offset, strip_width, 1)
    top_diag = diag_blocks[0] - product(fill_all, fill_strip)
    own_arrow = lax.dynamic_slice_in_dim(arrow_blocks[0], offset, strip_width, 1)
    own_arrow = own_arrow - product(branch_solved, fill_strip)
    next_arrow = -product(branch_solved, link_strip)
    came_arrow = shifted(next_arrow, "tm", 1)
    next_diag = -product(link_all, link_strip)
    next_upper = -product(fill_all, link_strip)
    stacked = jnp.stack([top_diag, next_diag, next_upper])[None]
    tip_all, came_arrow, stacked = lax.optimization_barrier((tip_all, came_arrow, stacked))
    spread = lax.all_to_all(stacked, "tm", split_axis=2, concat_axis=0, tiled=True)
    zero = jnp.zeros_like(spread[:1, 1])
    before = jnp.concatenate([zero, spread[:parts - 1, 1]], axis=0)
    red_diag = spread[:, 0] + before
    red_upper = jnp.concatenate([zero, spread[:parts - 1, 2]], axis=0)
    red_tip = tip_block + jnp.sum(tip_all, axis=0)
    red_arrow = (own_arrow + came_arrow)[None]
    return (red_diag, red_upper, red_arrow, red_tip)


def solution(mesh):
    return jax.shard_map(
        body,
        mesh=mesh,
        in_specs=(P("tm", None, "tile"), P("tm", None, "tile"), P("tm", None, None), P()),
        out_specs=(P(None, "tm", "tile"), P(None, "tm", "tile"), P("tm", None, "tile"), P()),
        check_vma=False,
    )
```

```python
import jax
import jax.numpy as jnp
from jax import lax
from jax.sharding import PartitionSpec as P
from jax.experimental import pallas as pl
from jax.experimental.pallas import tpu as pltpu

precise = lax.Precision.HIGHEST
BLOCK = 128
INTERPRET = False


def shifted(value, axis, by):
    count = lax.axis_size(axis)
    pairs = [(i, i + by) for i in range(count) if 0 <= i + by < count]
    return lax.ppermute(value, axis, pairs)


def mm(left, right):
    return jnp.dot(left, right, precision=precise)


def product(left, right):
    return jnp.dot(left.T, right, precision=precise)


def chip_pair(strips):
    tile = lax.axis_index("tile")
    count = lax.axis_size("tile")
    far = lax.ppermute(strips, "tile", [(j, j ^ 2) for j in range(count)])
    upper_chip = tile // 2 == 1
    low = jnp.where(upper_chip, far, strips)
    high = jnp.where(upper_chip, strips, far)
    return jnp.stack([low, high])


def join_cores(mine):
    tile = lax.axis_index("tile")
    count = lax.axis_size("tile")
    other = lax.ppermute(mine, "tile", [(j, j ^ 1) for j in range(count)])
    second_core = tile % 2 == 1
    first = jnp.where(second_core, other, mine)
    second = jnp.where(second_core, mine, other)
    return jnp.concatenate([first[0], second[0], first[1], second[1]], axis=-1)


def full_columns(strips):
    return join_cores(chip_pair(strips))


def chol_inv_kernel(a_ref, lt_ref, inv_ref, work_ref):
    size = a_ref.shape[0]
    work_ref[...] = a_ref[...]
    eye = (lax.broadcasted_iota(jnp.int32, (size, size), 0)
           == lax.broadcasted_iota(jnp.int32, (size, size), 1))
    inv_ref[...] = eye.astype(jnp.float32)
    cols = lax.broadcasted_iota(jnp.int32, (1, size), 1)
    for j in range(size):
        top = (j // 8) * 8
        rows = lax.broadcasted_iota(jnp.int32, (size - top, 1), 0) + top
        scale = lax.rsqrt(work_ref[j:j + 1, j:j + 1])
        col = jnp.where(rows >= j, work_ref[top:, j:j + 1] * scale, 0.0)
        row = jnp.where(cols >= j, work_ref[j:j + 1, :] * scale, 0.0)
        lt_ref[j:j + 1, :] = row
        work_ref[top:, :] = work_ref[top:, :] - col * row
        inv_row = inv_ref[j:j + 1, :]
        weight = jnp.where(rows > j, col * scale, jnp.where(rows == j, 1.0 - scale, 0.0))
        inv_ref[top:, :] = inv_ref[top:, :] - weight * inv_row


def chol_inv(block):
    size = block.shape[0]
    shape = jax.ShapeDtypeStruct((size, size), jnp.float32)
    return pl.pallas_call(
        chol_inv_kernel,
        out_shape=(shape, shape),
        scratch_shapes=[pltpu.VMEM((size, size), jnp.float32)],
        interpret=INTERPRET,
    )(block)


def factor_blocks(pivot, riders, hooks):
    size = pivot.shape[0]
    inverses, panels = [], []
    rest = pivot
    for step, start in enumerate(range(0, size, BLOCK)):
        corner = rest[:BLOCK, :BLOCK]
        _, head_inv = chol_inv((corner + corner.T) * 0.5)
        if step in hooks:
            head_inv, riders = lax.optimization_barrier((head_inv, riders))
            riders = hooks[step](riders)
        inverses.append(head_inv)
        if start + BLOCK < size:
            below = mm(rest[BLOCK:, :BLOCK], head_inv.T)
            panels.append(below)
            rest = rest[BLOCK:, BLOCK:] - mm(below, below.T)
    return inverses, panels, riders


def forward_solve(inverses, panels, rhs):
    solved = []
    rest = rhs
    for step, head_inv in enumerate(inverses):
        part = mm(head_inv, rest[:BLOCK])
        solved.append(part)
        if step < len(panels):
            rest = rest[BLOCK:] - mm(panels[step], part)
    return jnp.concatenate(solved, axis=0)


def body(diag_blocks, upper_blocks, arrow_blocks, tip_block):
    strip_width = diag_blocks.shape[2]
    nodes = diag_blocks.shape[1]
    parts = lax.axis_size("tm")
    offset = lax.axis_index("tile") * strip_width
    whole_pivot = full_columns(diag_blocks[1])
    hooks = {
        0: lambda r: (chip_pair(r[0]), shifted(r[1], "tm", -1)),
        2: lambda r: (join_cores(r[0]), chip_pair(r[1])),
        4: lambda r: (r[0], join_cores(r[1])),
    }
    inverses, panels, riders = factor_blocks(
        whole_pivot, (upper_blocks[1], upper_blocks[0]), hooks)
    first_full, next_full = riders
    branch_solved = forward_solve(inverses, panels, arrow_blocks[1].T)
    tip_part = -product(branch_solved, branch_solved)
    tip_all = lax.all_gather(tip_part, "tm")
    rhs = jnp.concatenate([first_full.T, next_full], axis=1)
    solved = forward_solve(inverses, panels, rhs)
    fill_all = solved[:, :nodes]
    link_all = solved[:, nodes:]
    fill_strip = lax.dynamic_slice_in_dim(fill_all, offset, strip_width, 1)
    link_strip = lax.dynamic_slice_in_dim(link_all, offset, strip_width, 1)
    top_diag = diag_blocks[0] - product(fill_all, fill_strip)
    own_arrow = lax.dynamic_slice_in_dim(arrow_blocks[0], offset, strip_width, 1)
    own_arrow = own_arrow - product(branch_solved, fill_strip)
    next_arrow = -product(branch_solved, link_strip)
    came_arrow = shifted(next_arrow, "tm", 1)
    next_diag = -product(link_all, link_strip)
    next_upper = -product(fill_all, link_strip)
    stacked = jnp.stack([top_diag, next_diag, next_upper])[None]
    tip_all, stacked = lax.optimization_barrier((tip_all, stacked))
    spread = lax.all_to_all(stacked, "tm", split_axis=2, concat_axis=0, tiled=True)
    zero = jnp.zeros_like(spread[:1, 1])
    before = jnp.concatenate([zero, spread[:parts - 1, 1]], axis=0)
    red_diag = spread[:, 0] + before
    red_upper = jnp.concatenate([zero, spread[:parts - 1, 2]], axis=0)
    red_tip = tip_block + jnp.sum(tip_all, axis=0)
    red_arrow = (own_arrow + came_arrow)[None]
    return (red_diag, red_upper, red_arrow, red_tip)


def solution(mesh):
    return jax.shard_map(
        body,
        mesh=mesh,
        in_specs=(P("tm", None, "tile"), P("tm", None, "tile"), P("tm", None, None), P()),
        out_specs=(P(None, "tm", "tile"), P(None, "tm", "tile"), P("tm", None, "tile"), P()),
        check_vma=False,
    )
```

```python
import jax
import jax.numpy as jnp
from jax import lax
from jax.sharding import PartitionSpec as P
from jax.experimental import pallas as pl
from jax.experimental.pallas import tpu as pltpu

precise = lax.Precision.HIGHEST
BLOCK = 128
INTERPRET = False


def shifted(value, axis, by):
    count = lax.axis_size(axis)
    pairs = [(i, i + by) for i in range(count) if 0 <= i + by < count]
    return lax.ppermute(value, axis, pairs)


def mm(left, right):
    return jnp.dot(left, right, precision=precise)


def product(left, right):
    return jnp.dot(left.T, right, precision=precise)


def chip_pair(strips):
    tile = lax.axis_index("tile")
    count = lax.axis_size("tile")
    far = lax.ppermute(strips, "tile", [(j, j ^ 2) for j in range(count)])
    upper_chip = tile // 2 == 1
    low = jnp.where(upper_chip, far, strips)
    high = jnp.where(upper_chip, strips, far)
    return jnp.stack([low, high])


def join_cores(mine):
    tile = lax.axis_index("tile")
    count = lax.axis_size("tile")
    other = lax.ppermute(mine, "tile", [(j, j ^ 1) for j in range(count)])
    second_core = tile % 2 == 1
    first = jnp.where(second_core, other, mine)
    second = jnp.where(second_core, mine, other)
    return jnp.concatenate([first[0], second[0], first[1], second[1]], axis=-1)


def full_columns(strips):
    return join_cores(chip_pair(strips))


def chol_inv_kernel(a_ref, lt_ref, inv_ref, work_ref):
    size = a_ref.shape[0]
    work_ref[...] = a_ref[...]
    eye = (lax.broadcasted_iota(jnp.int32, (size, size), 0)
           == lax.broadcasted_iota(jnp.int32, (size, size), 1))
    inv_ref[...] = eye.astype(jnp.float32)
    cols = lax.broadcasted_iota(jnp.int32, (1, size), 1)
    for j in range(size):
        top = (j // 8) * 8
        rows = lax.broadcasted_iota(jnp.int32, (size - top, 1), 0) + top
        scale = lax.rsqrt(work_ref[j:j + 1, j:j + 1])
        col = jnp.where(rows >= j, work_ref[top:, j:j + 1] * scale, 0.0)
        row = jnp.where(cols >= j, work_ref[j:j + 1, :] * scale, 0.0)
        lt_ref[j:j + 1, :] = row
        work_ref[top:, :] = work_ref[top:, :] - col * row
        inv_row = inv_ref[j:j + 1, :]
        weight = jnp.where(rows > j, col * scale, jnp.where(rows == j, 1.0 - scale, 0.0))
        inv_ref[top:, :] = inv_ref[top:, :] - weight * inv_row


def chol_inv(block):
    size = block.shape[0]
    shape = jax.ShapeDtypeStruct((size, size), jnp.float32)
    return pl.pallas_call(
        chol_inv_kernel,
        out_shape=(shape, shape),
        scratch_shapes=[pltpu.VMEM((size, size), jnp.float32)],
        interpret=INTERPRET,
    )(block)


def factor_blocks(pivot, riders, hooks):
    size = pivot.shape[0]
    inverses, panels = [], []
    rest = pivot
    for step, start in enumerate(range(0, size, BLOCK)):
        corner = rest[:BLOCK, :BLOCK]
        _, head_inv = chol_inv((corner + corner.T) * 0.5)
        if step in hooks:
            head_inv, riders = lax.optimization_barrier((head_inv, riders))
            riders = hooks[step](riders)
        inverses.append(head_inv)
        if start + BLOCK < size:
            below = mm(rest[BLOCK:, :BLOCK], head_inv.T)
            panels.append(below)
            rest = rest[BLOCK:, BLOCK:] - mm(below, below.T)
    return inverses, panels, riders


def forward_solve(inverses, panels, rhs):
    solved = []
    rest = rhs
    for step, head_inv in enumerate(inverses):
        part = mm(head_inv, rest[:BLOCK])
        solved.append(part)
        if step < len(panels):
            rest = rest[BLOCK:] - mm(panels[step], part)
    return jnp.concatenate(solved, axis=0)


def body(diag_blocks, upper_blocks, arrow_blocks, tip_block):
    strip_width = diag_blocks.shape[2]
    nodes = diag_blocks.shape[1]
    parts = lax.axis_size("tm")
    offset = lax.axis_index("tile") * strip_width
    whole_pivot = full_columns(diag_blocks[1])
    hooks = {
        0: lambda r: (chip_pair(r[0]), shifted(r[1], "tm", -1)),
        2: lambda r: (join_cores(r[0]), chip_pair(r[1])),
        4: lambda r: (r[0], join_cores(r[1])),
    }
    inverses, panels, riders = factor_blocks(
        whole_pivot, (upper_blocks[1], upper_blocks[0]), hooks)
    first_full, next_full = riders
    branch_solved = forward_solve(inverses, panels, arrow_blocks[1].T)
    tip_part = -product(branch_solved, branch_solved)
    tip_all = lax.all_gather(tip_part, "tm")
    link_all = forward_solve(inverses, panels, next_full)
    link_strip = lax.dynamic_slice_in_dim(link_all, offset, strip_width, 1)
    next_diag = -product(link_all, link_strip)
    next_arrow = -product(branch_solved, link_strip)
    next_diag, next_arrow, first_full = lax.optimization_barrier(
        (next_diag, next_arrow, first_full))
    came_diag, came_arrow = shifted((next_diag, next_arrow), "tm", 1)
    fill_all = forward_solve(inverses, panels, first_full.T)
    fill_strip = lax.dynamic_slice_in_dim(fill_all, offset, strip_width, 1)
    top_diag = diag_blocks[0] - product(fill_all, fill_strip)
    own_arrow = lax.dynamic_slice_in_dim(arrow_blocks[0], offset, strip_width, 1)
    own_arrow = own_arrow - product(branch_solved, fill_strip)
    next_upper = -product(fill_all, link_strip)
    stacked = jnp.stack([top_diag + came_diag, next_upper])[None]
    tip_all, stacked = lax.optimization_barrier((tip_all, stacked))
    spread = lax.all_to_all(stacked, "tm", split_axis=2, concat_axis=0, tiled=True)
    zero = jnp.zeros_like(spread[:1, 1])
    red_diag = spread[:, 0]
    red_upper = jnp.concatenate([zero, spread[:parts - 1, 1]], axis=0)
    red_tip = tip_block + jnp.sum(tip_all, axis=0)
    red_arrow = (own_arrow + came_arrow)[None]
    return (red_diag, red_upper, red_arrow, red_tip)


def solution(mesh):
    return jax.shard_map(
        body,
        mesh=mesh,
        in_specs=(P("tm", None, "tile"), P("tm", None, "tile"), P("tm", None, None), P()),
        out_specs=(P(None, "tm", "tile"), P(None, "tm", "tile"), P("tm", None, "tile"), P()),
        check_vma=False,
    )
```

```python
import jax
import jax.numpy as jnp
from jax import lax
from jax.sharding import PartitionSpec as P
from jax.experimental import pallas as pl
from jax.experimental.pallas import tpu as pltpu

precise = lax.Precision.HIGHEST
BLOCK = 128
INTERPRET = False


def shifted(value, axis, by):
    count = lax.axis_size(axis)
    pairs = [(i, i + by) for i in range(count) if 0 <= i + by < count]
    return lax.ppermute(value, axis, pairs)


def mm(left, right):
    return jnp.dot(left, right, precision=precise)


def product(left, right):
    return jnp.dot(left.T, right, precision=precise)


def chip_pair(strips):
    tile = lax.axis_index("tile")
    count = lax.axis_size("tile")
    far = lax.ppermute(strips, "tile", [(j, j ^ 2) for j in range(count)])
    upper_chip = tile // 2 == 1
    low = jnp.where(upper_chip, far, strips)
    high = jnp.where(upper_chip, strips, far)
    return jnp.stack([low, high])


def join_cores(mine):
    tile = lax.axis_index("tile")
    count = lax.axis_size("tile")
    other = lax.ppermute(mine, "tile", [(j, j ^ 1) for j in range(count)])
    second_core = tile % 2 == 1
    first = jnp.where(second_core, other, mine)
    second = jnp.where(second_core, mine, other)
    return jnp.concatenate([first[0], second[0], first[1], second[1]], axis=-1)


def full_columns(strips):
    return join_cores(chip_pair(strips))


def chol_inv_kernel(a_ref, lt_ref, inv_ref, work_ref):
    size = a_ref.shape[0]
    work_ref[...] = a_ref[...]
    eye = (lax.broadcasted_iota(jnp.int32, (size, size), 0)
           == lax.broadcasted_iota(jnp.int32, (size, size), 1))
    inv_ref[...] = eye.astype(jnp.float32)
    cols = lax.broadcasted_iota(jnp.int32, (1, size), 1)
    for j in range(size):
        top = (j // 8) * 8
        rows = lax.broadcasted_iota(jnp.int32, (size - top, 1), 0) + top
        scale = lax.rsqrt(work_ref[j:j + 1, j:j + 1])
        col = jnp.where(rows >= j, work_ref[top:, j:j + 1] * scale, 0.0)
        row = jnp.where(cols >= j, work_ref[j:j + 1, :] * scale, 0.0)
        lt_ref[j:j + 1, :] = row
        work_ref[top:, :] = work_ref[top:, :] - col * row
        inv_row = inv_ref[j:j + 1, :]
        weight = jnp.where(rows > j, col * scale, jnp.where(rows == j, 1.0 - scale, 0.0))
        inv_ref[top:, :] = inv_ref[top:, :] - weight * inv_row


def chol_inv(block):
    size = block.shape[0]
    shape = jax.ShapeDtypeStruct((size, size), jnp.float32)
    return pl.pallas_call(
        chol_inv_kernel,
        out_shape=(shape, shape),
        scratch_shapes=[pltpu.VMEM((size, size), jnp.float32)],
        interpret=INTERPRET,
    )(block)


def factor_blocks(pivot, riders, hooks):
    size = pivot.shape[0]
    inverses, panels = [], []
    rest = pivot
    for step, start in enumerate(range(0, size, BLOCK)):
        corner = rest[:BLOCK, :BLOCK]
        _, head_inv = chol_inv((corner + corner.T) * 0.5)
        if step in hooks:
            head_inv, riders = lax.optimization_barrier((head_inv, riders))
            riders = hooks[step](riders)
        inverses.append(head_inv)
        if start + BLOCK < size:
            below = mm(rest[BLOCK:, :BLOCK], head_inv.T)
            panels.append(below)
            rest = rest[BLOCK:, BLOCK:] - mm(below, below.T)
    return inverses, panels, riders


def forward_solve(inverses, panels, rhs):
    solved = []
    rest = rhs
    for step, head_inv in enumerate(inverses):
        part = mm(head_inv, rest[:BLOCK])
        solved.append(part)
        if step < len(panels):
            rest = rest[BLOCK:] - mm(panels[step], part)
    return jnp.concatenate(solved, axis=0)


def body(diag_blocks, upper_blocks, arrow_blocks, tip_block):
    strip_width = diag_blocks.shape[2]
    nodes = diag_blocks.shape[1]
    parts = lax.axis_size("tm")
    offset = lax.axis_index("tile") * strip_width
    whole_pivot = full_columns(diag_blocks[1])
    upper_after = shifted(upper_blocks[0], "tm", -1)
    hooks = {
        0: lambda r: (chip_pair(r[0]), upper_after),
        3: lambda r: (join_cores(r[0]), chip_pair(r[1])),
        5: lambda r: (r[0], join_cores(r[1])),
    }
    inverses, panels, riders = factor_blocks(whole_pivot, (upper_blocks[1],), hooks)
    first_full, next_full = riders
    branch_solved = forward_solve(inverses, panels, arrow_blocks[1].T)
    tip_part = -product(branch_solved, branch_solved)
    tip_all = lax.all_gather(tip_part, "tm")
    rhs = jnp.concatenate([first_full.T, next_full], axis=1)
    solved = forward_solve(inverses, panels, rhs)
    fill_all = solved[:, :nodes]
    link_all = solved[:, nodes:]
    fill_strip = lax.dynamic_slice_in_dim(fill_all, offset, strip_width, 1)
    link_strip = lax.dynamic_slice_in_dim(link_all, offset, strip_width, 1)
    top_diag = diag_blocks[0] - product(fill_all, fill_strip)
    own_arrow = lax.dynamic_slice_in_dim(arrow_blocks[0], offset, strip_width, 1)
    own_arrow = own_arrow - product(branch_solved, fill_strip)
    next_arrow = -product(branch_solved, link_strip)
    came_arrow = shifted(next_arrow, "tm", 1)
    next_diag = -product(link_all, link_strip)
    next_upper = -product(fill_all, link_strip)
    stacked = jnp.stack([top_diag, next_diag, next_upper])[None]
    tip_all, stacked = lax.optimization_barrier((tip_all, stacked))
    spread = lax.all_to_all(stacked, "tm", split_axis=2, concat_axis=0, tiled=True)
    zero = jnp.zeros_like(spread[:1, 1])
    before = jnp.concatenate([zero, spread[:parts - 1, 1]], axis=0)
    red_diag = spread[:, 0] + before
    red_upper = jnp.concatenate([zero, spread[:parts - 1, 2]], axis=0)
    red_tip = tip_block + jnp.sum(tip_all, axis=0)
    red_arrow = (own_arrow + came_arrow)[None]
    return (red_diag, red_upper, red_arrow, red_tip)


def solution(mesh):
    return jax.shard_map(
        body,
        mesh=mesh,
        in_specs=(P("tm", None, "tile"), P("tm", None, "tile"), P("tm", None, None), P()),
        out_specs=(P(None, "tm", "tile"), P(None, "tm", "tile"), P("tm", None, "tile"), P()),
        check_vma=False,
    )
```

```python
import jax
import jax.numpy as jnp
from jax import lax
from jax.sharding import PartitionSpec as P
from jax.experimental import pallas as pl
from jax.experimental.pallas import tpu as pltpu

precise = lax.Precision.HIGHEST
BLOCK = 128
INTERPRET = False


def shifted(value, axis, by):
    count = lax.axis_size(axis)
    pairs = [(i, i + by) for i in range(count) if 0 <= i + by < count]
    return lax.ppermute(value, axis, pairs)


def mm(left, right):
    return jnp.dot(left, right, precision=precise)


def product(left, right):
    return jnp.dot(left.T, right, precision=precise)


def chip_pair(strips):
    tile = lax.axis_index("tile")
    count = lax.axis_size("tile")
    far = lax.ppermute(strips, "tile", [(j, j ^ 2) for j in range(count)])
    upper_chip = tile // 2 == 1
    low = jnp.where(upper_chip, far, strips)
    high = jnp.where(upper_chip, strips, far)
    return jnp.stack([low, high])


def join_cores(mine):
    tile = lax.axis_index("tile")
    count = lax.axis_size("tile")
    other = lax.ppermute(mine, "tile", [(j, j ^ 1) for j in range(count)])
    second_core = tile % 2 == 1
    first = jnp.where(second_core, other, mine)
    second = jnp.where(second_core, mine, other)
    return jnp.concatenate([first[0], second[0], first[1], second[1]], axis=-1)


def full_columns(strips):
    return join_cores(chip_pair(strips))


def chol_inv_kernel(a_ref, inv_ref, work_ref):
    size = a_ref.shape[0]
    work_ref[...] = a_ref[...]
    eye = (lax.broadcasted_iota(jnp.int32, (size, size), 0)
           == lax.broadcasted_iota(jnp.int32, (size, size), 1))
    inv_ref[...] = eye.astype(jnp.float32)
    cols = lax.broadcasted_iota(jnp.int32, (1, size), 1)
    for j in range(size):
        top = (j // 8) * 8
        rows = lax.broadcasted_iota(jnp.int32, (size - top, 1), 0) + top
        scale = lax.rsqrt(work_ref[j:j + 1, j:j + 1])
        col = jnp.where(rows >= j, work_ref[top:, j:j + 1] * scale, 0.0)
        row = jnp.where(cols >= j, work_ref[j:j + 1, :] * scale, 0.0)
        work_ref[top:, :] = work_ref[top:, :] - col * row
        inv_row = inv_ref[j:j + 1, :]
        weight = jnp.where(rows > j, col * scale, jnp.where(rows == j, 1.0 - scale, 0.0))
        inv_ref[top:, :] = inv_ref[top:, :] - weight * inv_row


def chol_inv(block):
    size = block.shape[0]
    shape = jax.ShapeDtypeStruct((size, size), jnp.float32)
    return pl.pallas_call(
        chol_inv_kernel,
        out_shape=shape,
        scratch_shapes=[pltpu.VMEM((size, size), jnp.float32)],
        interpret=INTERPRET,
    )(block)


def factor_blocks(pivot, riders, hooks):
    size = pivot.shape[0]
    inverses, panels = [], []
    rest = pivot
    for step, start in enumerate(range(0, size, BLOCK)):
        corner = rest[:BLOCK, :BLOCK]
        head_inv = chol_inv(corner)
        if step in hooks:
            head_inv, riders = lax.optimization_barrier((head_inv, riders))
            riders = hooks[step](riders)
        inverses.append(head_inv)
        if start + BLOCK < size:
            below = mm(rest[BLOCK:, :BLOCK], head_inv.T)
            panels.append(below)
            rest = rest[BLOCK:, BLOCK:] - mm(below, below.T)
    return inverses, panels, riders


def forward_solve(inverses, panels, rhs):
    solved = []
    rest = rhs
    for step, head_inv in enumerate(inverses):
        part = mm(head_inv, rest[:BLOCK])
        solved.append(part)
        if step < len(panels):
            rest = rest[BLOCK:] - mm(panels[step], part)
    return jnp.concatenate(solved, axis=0)


def body(diag_blocks, upper_blocks, arrow_blocks, tip_block):
    strip_width = diag_blocks.shape[2]
    nodes = diag_blocks.shape[1]
    parts = lax.axis_size("tm")
    offset = lax.axis_index("tile") * strip_width
    whole_pivot = full_columns(diag_blocks[1])
    upper_after = shifted(upper_blocks[0], "tm", -1)
    hooks = {
        0: lambda r: (chip_pair(r[0]), upper_after),
        3: lambda r: (join_cores(r[0]), chip_pair(r[1])),
        5: lambda r: (r[0], join_cores(r[1])),
    }
    inverses, panels, riders = factor_blocks(whole_pivot, (upper_blocks[1],), hooks)
    first_full, next_full = riders
    branch_solved = forward_solve(inverses, panels, arrow_blocks[1].T)
    tip_part = -product(branch_solved, branch_solved)
    tip_all = lax.all_gather(tip_part, "tm")
    rhs = jnp.concatenate([first_full.T, next_full], axis=1)
    solved = forward_solve(inverses, panels, rhs)
    fill_all = solved[:, :nodes]
    link_all = solved[:, nodes:]
    fill_strip = lax.dynamic_slice_in_dim(fill_all, offset, strip_width, 1)
    link_strip = lax.dynamic_slice_in_dim(link_all, offset, strip_width, 1)
    top_diag = diag_blocks[0] - product(fill_all, fill_strip)
    own_arrow = lax.dynamic_slice_in_dim(arrow_blocks[0], offset, strip_width, 1)
    own_arrow = own_arrow - product(branch_solved, fill_strip)
    next_arrow = -product(branch_solved, link_strip)
    came_arrow = shifted(next_arrow, "tm", 1)
    next_diag = -product(link_all, link_strip)
    next_upper = -product(fill_all, link_strip)
    stacked = jnp.stack([top_diag, next_diag, next_upper])[None]
    tip_all, stacked = lax.optimization_barrier((tip_all, stacked))
    spread = lax.all_to_all(stacked, "tm", split_axis=2, concat_axis=0, tiled=True)
    zero = jnp.zeros_like(spread[:1, 1])
    before = jnp.concatenate([zero, spread[:parts - 1, 1]], axis=0)
    red_diag = spread[:, 0] + before
    red_upper = jnp.concatenate([zero, spread[:parts - 1, 2]], axis=0)
    red_tip = tip_block + jnp.sum(tip_all, axis=0)
    red_arrow = (own_arrow + came_arrow)[None]
    return (red_diag, red_upper, red_arrow, red_tip)


def solution(mesh):
    return jax.shard_map(
        body,
        mesh=mesh,
        in_specs=(P("tm", None, "tile"), P("tm", None, "tile"), P("tm", None, None), P()),
        out_specs=(P(None, "tm", "tile"), P(None, "tm", "tile"), P("tm", None, "tile"), P()),
        check_vma=False,
    )
```

```python
import jax
import jax.numpy as jnp
from jax import lax
from jax.sharding import PartitionSpec as P
from jax.experimental import pallas as pl
from jax.experimental.pallas import tpu as pltpu

precise = lax.Precision.HIGHEST
BLOCK = 128
INTERPRET = False


def shifted(value, axis, by):
    count = lax.axis_size(axis)
    pairs = [(i, i + by) for i in range(count) if 0 <= i + by < count]
    return lax.ppermute(value, axis, pairs)


def mm(left, right):
    return jnp.dot(left, right, precision=precise)


def product(left, right):
    return jnp.dot(left.T, right, precision=precise)


def chip_pair(strips):
    tile = lax.axis_index("tile")
    count = lax.axis_size("tile")
    far = lax.ppermute(strips, "tile", [(j, j ^ 2) for j in range(count)])
    upper_chip = tile // 2 == 1
    low = jnp.where(upper_chip, far, strips)
    high = jnp.where(upper_chip, strips, far)
    return jnp.stack([low, high])


def join_cores(mine):
    tile = lax.axis_index("tile")
    count = lax.axis_size("tile")
    other = lax.ppermute(mine, "tile", [(j, j ^ 1) for j in range(count)])
    second_core = tile % 2 == 1
    first = jnp.where(second_core, other, mine)
    second = jnp.where(second_core, mine, other)
    return jnp.concatenate([first[0], second[0], first[1], second[1]], axis=-1)


def full_columns(strips):
    return join_cores(chip_pair(strips))


def chol_inv_kernel(a_ref, inv_ref, work_ref):
    size = a_ref.shape[0]
    work_ref[...] = a_ref[...]
    eye = (lax.broadcasted_iota(jnp.int32, (size, size), 0)
           == lax.broadcasted_iota(jnp.int32, (size, size), 1))
    inv_ref[...] = eye.astype(jnp.float32)
    cols = lax.broadcasted_iota(jnp.int32, (1, size), 1)
    for j in range(size):
        top = (j // 8) * 8
        rows = lax.broadcasted_iota(jnp.int32, (size - top, 1), 0) + top
        scale = lax.rsqrt(work_ref[j:j + 1, j:j + 1])
        col = jnp.where(rows >= j, work_ref[top:, j:j + 1] * scale, 0.0)
        row = jnp.where(cols >= j, work_ref[j:j + 1, :] * scale, 0.0)
        work_ref[top:, :] = work_ref[top:, :] - col * row
        inv_row = inv_ref[j:j + 1, :]
        weight = jnp.where(rows > j, col * scale, jnp.where(rows == j, 1.0 - scale, 0.0))
        inv_ref[top:, :] = inv_ref[top:, :] - weight * inv_row


def chol_inv(matrix, size):
    shape = jax.ShapeDtypeStruct((size, size), jnp.float32)
    return pl.pallas_call(
        chol_inv_kernel,
        out_shape=shape,
        grid=(1,),
        in_specs=[pl.BlockSpec((size, size), lambda i: (0, 0))],
        out_specs=pl.BlockSpec((size, size), lambda i: (0, 0)),
        scratch_shapes=[pltpu.VMEM((size, size), jnp.float32)],
        interpret=INTERPRET,
    )(matrix)


def factor_blocks(pivot, riders, hooks):
    size = pivot.shape[0]
    inverses, panels = [], []
    rest = pivot
    for step, start in enumerate(range(0, size, BLOCK)):
        head_inv = chol_inv(rest, BLOCK)
        if step in hooks:
            head_inv, riders = lax.optimization_barrier((head_inv, riders))
            riders = hooks[step](riders)
        inverses.append(head_inv)
        if start + BLOCK < size:
            below = mm(rest[BLOCK:, :BLOCK], head_inv.T)
            panels.append(below)
            rest = rest[BLOCK:, BLOCK:] - mm(below, below.T)
    return inverses, panels, riders


def forward_solve(inverses, panels, rhs):
    solved = []
    rest = rhs
    for step, head_inv in enumerate(inverses):
        part = mm(head_inv, rest[:BLOCK])
        solved.append(part)
        if step < len(panels):
            rest = rest[BLOCK:] - mm(panels[step], part)
    return jnp.concatenate(solved, axis=0)


def body(diag_blocks, upper_blocks, arrow_blocks, tip_block):
    strip_width = diag_blocks.shape[2]
    nodes = diag_blocks.shape[1]
    parts = lax.axis_size("tm")
    offset = lax.axis_index("tile") * strip_width
    whole_pivot = full_columns(diag_blocks[1])
    upper_after = shifted(upper_blocks[0], "tm", -1)
    hooks = {
        0: lambda r: (chip_pair(r[0]), upper_after),
        3: lambda r: (join_cores(r[0]), chip_pair(r[1])),
        5: lambda r: (r[0], join_cores(r[1])),
    }
    inverses, panels, riders = factor_blocks(whole_pivot, (upper_blocks[1],), hooks)
    first_full, next_full = riders
    branch_solved = forward_solve(inverses, panels, arrow_blocks[1].T)
    tip_part = -product(branch_solved, branch_solved)
    tip_all = lax.all_gather(tip_part, "tm")
    rhs = jnp.concatenate([first_full.T, next_full], axis=1)
    solved = forward_solve(inverses, panels, rhs)
    fill_all = solved[:, :nodes]
    link_all = solved[:, nodes:]
    fill_strip = lax.dynamic_slice_in_dim(fill_all, offset, strip_width, 1)
    link_strip = lax.dynamic_slice_in_dim(link_all, offset, strip_width, 1)
    top_diag = diag_blocks[0] - product(fill_all, fill_strip)
    own_arrow = lax.dynamic_slice_in_dim(arrow_blocks[0], offset, strip_width, 1)
    own_arrow = own_arrow - product(branch_solved, fill_strip)
    next_arrow = -product(branch_solved, link_strip)
    came_arrow = shifted(next_arrow, "tm", 1)
    next_diag = -product(link_all, link_strip)
    next_upper = -product(fill_all, link_strip)
    stacked = jnp.stack([top_diag, next_diag, next_upper])[None]
    tip_all, stacked = lax.optimization_barrier((tip_all, stacked))
    spread = lax.all_to_all(stacked, "tm", split_axis=2, concat_axis=0, tiled=True)
    zero = jnp.zeros_like(spread[:1, 1])
    before = jnp.concatenate([zero, spread[:parts - 1, 1]], axis=0)
    red_diag = spread[:, 0] + before
    red_upper = jnp.concatenate([zero, spread[:parts - 1, 2]], axis=0)
    red_tip = tip_block + jnp.sum(tip_all, axis=0)
    red_arrow = (own_arrow + came_arrow)[None]
    return (red_diag, red_upper, red_arrow, red_tip)


def solution(mesh):
    return jax.shard_map(
        body,
        mesh=mesh,
        in_specs=(P("tm", None, "tile"), P("tm", None, "tile"), P("tm", None, None), P()),
        out_specs=(P(None, "tm", "tile"), P(None, "tm", "tile"), P("tm", None, "tile"), P()),
        check_vma=False,
    )
```
